256 devices in a mesh: col: 32 (over z, x), row: 8 (over y, core).
Axes of the slice: x: 4, y: 4, z: 8, core: 2. Of those that a mesh axis runs over, the one named last changes fastest.
Arguments:
- right_side: float32 [6, 64, 64, 128], P(None, 'row'), may hold values from -6 to 6
- lower_blocks: bfloat16 [15, 64, 64, 128, 128], P(None, 'row', 'col'), may hold values from -0.078125 to 0.078125
- pattern: int32 [15, 64, 64], P(None, 'row', 'col'), may hold values 0 or 1
- diag_inverse: bfloat16 [6, 64, 128, 128], P(None, 'row'), may hold values from -2 to 2
Outputs:
- solution: float32 [6, 64, 64, 128], P(None, 'col')
The draws below stay inside these ranges and needn't reach their ends.
All inputs are finite; a program needn't handle non-finite values. No bound on the sum of `pattern` on one device may be relied on, other than what follows from the above.
Results may differ from the reference program's by a relative error of at most 0.0029.
Values sent between devices are 32-bit elements; how exact they have to be, the bound alone decides.
No kernel may reach another device: no remote copies, remote signals or barrier semaphores. Data moves between devices by JAX's collectives and lax.ppermute only.
A program may use at most 64 MiB of HBM per device.

```python
import math
import jax
import jax.numpy as jnp
from jax import lax

B = 128
NRHS = 64
LEVELS = 6
P_SIZE = 64
PAIRS = 15


def draw_diag_inverse(key, part):
    key_off, key_dia = jax.random.split(jax.random.fold_in(key, 17))
    off_part = jax.random.normal(key_off, (LEVELS, P_SIZE, B, B), jnp.float32) * (0.6 / math.sqrt(B))
    dia_part = jax.random.uniform(key_dia, (LEVELS, P_SIZE, B), jnp.float32, 0.5, 1.5)
    off_part = jnp.clip(off_part, -0.15, 0.15)
    identity = jnp.eye(B, dtype=jnp.float32)
    return (off_part + dia_part[..., :, None] * identity).astype(jnp.bfloat16)


def touch_ends(values, rng, least, high):
    dims = values.shape
    spot = [jax.random.randint(jax.random.fold_in(rng, axis), (), 0, dims[axis]) for axis in range(len(dims))]
    values = values.at[tuple(spot)].set(least)
    longest = dims.index(max(dims))
    spot[longest] = (spot[longest] + 1) % dims[longest]
    return values.at[tuple(spot)].set(high)


def with_spikes(values, own_key, source, target, blocks, factor):
    def block_of(position):
        return (jnp.arange(values.shape[position]) // (values.shape[position] // blocks)).reshape((-1,) + (1,) * (values.ndim - 1 - position))

    one_side = jax.random.permutation(own_key, blocks)[block_of(target)]
    second = (block_of(target) + blocks // 2) % blocks
    return jnp.where((block_of(source) == one_side) | (block_of(source) == second), factor * values, values)


def level_of(own_key, shape, pieces, least, high):
    level = 1.0
    for position, blocks in pieces:
        heights = jax.random.uniform(jax.random.fold_in(jax.random.fold_in(own_key, 6), position), (blocks,), jnp.float32, least / len(pieces), high / len(pieces))
        level = level * jnp.repeat(jnp.exp(heights), shape[position] // blocks).reshape((-1,) + (1,) * (len(shape) - 1 - position))
    return level


def noise(rng, dims, deviation, limit, cuts=(), held_as=jnp.bfloat16):
    values = deviation * jax.random.normal(rng, dims, jnp.float32)
    if cuts:
        values = values * level_of(rng, dims, cuts, -0.22, 0.18)
    return jnp.clip(values, -limit, limit).astype(held_as)


def noise_with(own_key, shape, width, limit, cuts, heavy, kind=jnp.bfloat16):
    values = width * jax.random.normal(own_key, shape, jnp.float32)
    if cuts:
        values = values * level_of(own_key, shape, cuts, -0.22, 0.18)
    return jnp.clip(with_spikes(values, jax.random.fold_in(own_key, 3), *heavy), -limit, limit).astype(kind)


def setup_inputs(seed: int = 0) -> dict:
    key_list = jax.random.split(jax.random.key(seed), 5)
    right_side = noise(key_list[0], (LEVELS, P_SIZE, NRHS, B), 1.0, 6.0, ((1, 8),), jnp.float32)
    lower_blocks = noise_with(key_list[1], (PAIRS, P_SIZE, P_SIZE, B, B), (P_SIZE * B * LEVELS // 2) ** -0.5, 0.078125, ((1, 8), (2, 32)), (2, 1, 32, 2.75))
    pattern = touch_ends((jax.random.randint(key_list[2], (PAIRS, P_SIZE, P_SIZE), 0, 2) < 1).astype(jnp.int32), jax.random.fold_in(key_list[2], 1), 0, 1)
    diag_inverse = draw_diag_inverse(jax.random.fold_in(key_list[4], 71), 0)
    return dict(right_side=right_side, lower_blocks=lower_blocks, pattern=pattern, diag_inverse=diag_inverse)


def reference(right_side, lower_blocks, pattern, diag_inverse):
    solved = []
    outputs = []
    for section in range(LEVELS):
        residual = right_side[section]
        if section > 0:
            offset = section * (section - 1) // 2
            contrib = jnp.zeros((P_SIZE, NRHS, B), jnp.float32)
            for prior in range(section):
                blocks = lower_blocks[offset + prior].astype(jnp.float32)
                weights = pattern[offset + prior].astype(jnp.float32)
                earlier = solved[prior].astype(jnp.float32)
                products = jnp.einsum("cnb,rcbd->rcnd", earlier, blocks, precision=lax.Precision.HIGHEST)
                contrib = contrib + jnp.sum(weights[:, :, None, None] * products, axis=1)
            residual = residual - contrib
        inverse = diag_inverse[section].astype(jnp.float32)
        solution = jnp.einsum("pnb,pbd->pnd", residual, inverse, precision=lax.Precision.HIGHEST)
        outputs.append(solution)
        solved.append(solution.astype(jnp.bfloat16))
    return jnp.stack(outputs)
```

```python
import jax
import jax.numpy as jnp
from jax import lax
from jax.sharding import PartitionSpec as P


def solve_rows(residual, inverse):
    return jnp.einsum(
        "pnb,pbd->pnd", residual, inverse.astype(jnp.float32), precision=lax.Precision.HIGHEST
    )


def make_body(n_col, n_row):
    def body(right_side, lower_blocks, pattern, diag_inverse):
        row_count = right_side.shape[1]
        col_count = pattern.shape[2]
        groups = row_count // col_count
        planes = n_col // groups
        col_id = lax.axis_index("col")
        row_id = lax.axis_index("row")
        x_id = col_id % groups
        z_id = col_id // groups
        is_root = z_id == row_id
        axes = ("col", "row")

        def lin(c, r):
            return c * n_row + r

        def reduce_to_root(partial_value):
            pieces = partial_value.reshape((groups, col_count) + partial_value.shape[1:])
            acc = lax.dynamic_index_in_dim(pieces, x_id, 0, keepdims=False)
            for s in range(1, groups):
                send = lax.dynamic_index_in_dim(pieces, (x_id + s) % groups, 0, keepdims=False)
                perm = [
                    (zz * groups + xx, zz * groups + (xx + s) % groups)
                    for zz in range(planes)
                    for xx in range(groups)
                ]
                acc = acc + lax.ppermute(send, "col", perm)
            total = acc
            for s in range(1, planes):
                perm = [
                    (lin(((r + s) % planes) * groups + xx, r), lin(r * groups + xx, r))
                    for r in range(n_row)
                    for xx in range(groups)
                ]
                total = total + lax.ppermute(acc, axes, perm)
            return total

        def broadcast_from_root(owned):
            got = jnp.zeros_like(owned)
            for t in range(1, n_row):
                perm = [
                    (lin(z0 * groups + xx, z0), lin(z0 * groups + xx, (z0 + t) % n_row))
                    for z0 in range(planes)
                    for xx in range(groups)
                ]
                got = got + lax.ppermute(owned, axes, perm)
            return jnp.where(is_root, owned, got)

        solved = []
        outputs = []
        for section in range(right_side.shape[0]):
            rhs_owned = lax.dynamic_slice_in_dim(right_side[section], x_id * col_count, col_count, 0)
            inv_owned = lax.dynamic_slice_in_dim(diag_inverse[section], x_id * col_count, col_count, 0)
            if section > 0:
                offset = section * (section - 1) // 2
                blocks = lower_blocks[offset : offset + section]
                weights = pattern[offset : offset + section].astype(jnp.float32)
                earlier = jnp.stack(solved)
                products = jnp.einsum(
                    "lcnb,lrcbd->lrcnd", earlier, blocks, preferred_element_type=jnp.float32
                )
                partial_value = jnp.sum(weights[:, :, :, None, None] * products, axis=(0, 2))
                totals = reduce_to_root(partial_value)
                owned = solve_rows(rhs_owned - totals, inv_owned)
            else:
                owned = solve_rows(rhs_owned, inv_owned)
            segment = broadcast_from_root(owned)
            outputs.append(segment)
            solved.append(segment.astype(jnp.bfloat16))
        return jnp.stack(outputs)

    return body


def solution(mesh):
    placed = (
        P(None, "row", None, None),
        P(None, "row", "col", None, None),
        P(None, "row", "col"),
        P(None, "row", None, None),
    )
    body = make_body(mesh.shape["col"], mesh.shape["row"])
    return jax.shard_map(
        body, mesh=mesh, in_specs=placed, out_specs=P(None, "col", None, None), check_vma=False
    )
```

```python
import jax
import jax.numpy as jnp
from jax import lax
from jax.sharding import PartitionSpec as P


def solve_rows(residual, inverse):
    return jnp.einsum(
        "pnb,pbd->pnd", residual, inverse.astype(jnp.float32), precision=lax.Precision.HIGHEST
    )


def contributions(earlier, blocks, weights):
    products = jnp.einsum("lcnb,lrcbd->lrcnd", earlier, blocks, preferred_element_type=jnp.float32)
    return jnp.sum(weights[:, :, :, None, None] * products, axis=(0, 2))


def make_body(n_col, n_row):
    def body(right_side, lower_blocks, pattern, diag_inverse):
        row_count = right_side.shape[1]
        col_count = pattern.shape[2]
        groups = row_count // col_count
        planes = n_col // groups
        col_id = lax.axis_index("col")
        row_id = lax.axis_index("row")
        x_id = col_id % groups
        z_id = col_id // groups
        is_root = z_id == row_id
        axes = ("col", "row")

        def lin(c, r):
            return c * n_row + r

        def reduce_x(partial_value):
            pieces = partial_value.reshape((groups, col_count) + partial_value.shape[1:])
            acc = lax.dynamic_index_in_dim(pieces, x_id, 0, keepdims=False)
            for s in range(1, groups):
                send = lax.dynamic_index_in_dim(pieces, (x_id + s) % groups, 0, keepdims=False)
                perm = [
                    (zz * groups + xx, zz * groups + (xx + s) % groups)
                    for zz in range(planes)
                    for xx in range(groups)
                ]
                acc = acc + lax.ppermute(send, "col", perm)
            return acc

        def deliver(piece, shifts):
            got = None
            for t in range(shifts):
                perm = [
                    (lin(b * groups + xx, a), lin(a * groups + xx, (b + t) % n_row))
                    for a in range(n_row)
                    for b in range(planes)
                    for xx in range(groups)
                ]
                recv = lax.ppermute(piece, axes, perm)
                got = recv if got is None else got + recv
            return got

        solved = []
        outputs = []
        for section in range(right_side.shape[0]):
            rhs_owned = lax.dynamic_slice_in_dim(right_side[section], x_id * col_count, col_count, 0)
            inv_owned = lax.dynamic_slice_in_dim(diag_inverse[section], x_id * col_count, col_count, 0)
            if section > 0:
                offset = section * (section - 1) // 2
                weights = pattern[offset : offset + section].astype(jnp.float32)
                blocks = lower_blocks[offset : offset + section]
                partial_value = contributions(
                    jnp.stack(solved[-1:]), blocks[section - 1 :], weights[section - 1 :]
                )
                if section > 1:
                    partial_value = partial_value + contributions(
                        jnp.stack(solved[:-1]), blocks[: section - 1], weights[: section - 1]
                    )
                acc = reduce_x(partial_value)
                residual = jnp.where(is_root, rhs_owned, jnp.zeros_like(rhs_owned)) - acc
                segment = deliver(solve_rows(residual, inv_owned), planes)
            else:
                segment = deliver(solve_rows(rhs_owned, inv_owned), 1)
            outputs.append(segment)
            solved.append(segment.astype(jnp.bfloat16))
        return jnp.stack(outputs)

    return body


def solution(mesh):
    placed = (
        P(None, "row", None, None),
        P(None, "row", "col", None, None),
        P(None, "row", "col"),
        P(None, "row", None, None),
    )
    body = make_body(mesh.shape["col"], mesh.shape["row"])
    return jax.shard_map(
        body, mesh=mesh, in_specs=placed, out_specs=P(None, "col", None, None), check_vma=False
    )
```

```python
import jax
import jax.numpy as jnp
from jax import lax
from jax.sharding import PartitionSpec as P


def solve_rows(residual, inverse):
    return jnp.einsum(
        "pnb,pbd->pnd", residual, inverse.astype(jnp.float32), precision=lax.Precision.HIGHEST
    )


def contributions(earlier, blocks, weights):
    products = jnp.einsum("lcnb,lrcbd->lrcnd", earlier, blocks, preferred_element_type=jnp.float32)
    return jnp.sum(weights[:, :, :, None, None] * products, axis=(0, 2))


def make_body(n_col, n_row):
    def body(right_side, lower_blocks, pattern, diag_inverse):
        row_count = right_side.shape[1]
        nrhs = right_side.shape[2]
        width = right_side.shape[3]
        col_count = pattern.shape[2]
        groups = row_count // col_count
        planes = n_col // groups
        band = nrhs // planes
        col_id = lax.axis_index("col")
        x_id = col_id % groups
        z_id = col_id // groups

        def lin(c, r):
            return c * n_row + r

        transpose = [
            (lin(b * groups + xx, a), lin(a * groups + xx, b))
            for a in range(n_row)
            for b in range(planes)
            for xx in range(groups)
        ]

        def reduce_col(partial_value):
            pieces = partial_value.reshape(groups, col_count, planes, band, width)
            parts = pieces.transpose(2, 0, 1, 3, 4).reshape(n_col, col_count, band, width)
            got = lax.all_to_all(parts, "col", 0, 0, tiled=True)
            return jnp.sum(got, axis=0)

        def deliver(piece):
            moved = lax.ppermute(piece, ("col", "row"), transpose)
            copies = jnp.broadcast_to(moved[None], (n_row,) + moved.shape)
            got = lax.all_to_all(copies, "row", 0, 0, tiled=True)
            return got.transpose(1, 0, 2, 3).reshape(col_count, nrhs, width)

        solved = []
        outputs = []
        for section in range(right_side.shape[0]):
            rhs_owned = lax.dynamic_slice(
                right_side[section], (x_id * col_count, z_id * band, 0), (col_count, band, width)
            )
            inv_owned = lax.dynamic_slice_in_dim(diag_inverse[section], x_id * col_count, col_count, 0)
            if section > 0:
                offset = section * (section - 1) // 2
                weights = pattern[offset : offset + section].astype(jnp.float32)
                blocks = lower_blocks[offset : offset + section]
                partial_value = contributions(
                    jnp.stack(solved[-1:]), blocks[section - 1 :], weights[section - 1 :]
                )
                if section > 1:
                    partial_value = partial_value + contributions(
                        jnp.stack(solved[:-1]), blocks[: section - 1], weights[: section - 1]
                    )
                residual = rhs_owned - reduce_col(partial_value)
            else:
                residual = rhs_owned
            segment = deliver(solve_rows(residual, inv_owned))
            outputs.append(segment)
            solved.append(segment.astype(jnp.bfloat16))
        return jnp.stack(outputs)

    return body


def solution(mesh):
    placed = (
        P(None, "row", None, None),
        P(None, "row", "col", None, None),
        P(None, "row", "col"),
        P(None, "row", None, None),
    )
    body = make_body(mesh.shape["col"], mesh.shape["row"])
    return jax.shard_map(
        body, mesh=mesh, in_specs=placed, out_specs=P(None, "col", None, None), check_vma=False
    )
```

```python
import jax
import jax.numpy as jnp
from jax import lax
from jax.sharding import PartitionSpec as P


def solve_rows(residual, inverse):
    return jnp.einsum(
        "pnb,pbd->pnd", residual, inverse.astype(jnp.float32), precision=lax.Precision.HIGHEST
    )


def contributions(earlier, blocks, weights):
    products = jnp.einsum("lcnb,lrcbd->lrcnd", earlier, blocks, preferred_element_type=jnp.float32)
    return jnp.sum(weights[:, :, :, None, None] * products, axis=(0, 2))


def make_body(n_col, n_row):
    def body(right_side, lower_blocks, pattern, diag_inverse):
        row_count = right_side.shape[1]
        nrhs = right_side.shape[2]
        width = right_side.shape[3]
        col_count = pattern.shape[2]
        groups = row_count // col_count
        planes = n_col // groups
        band = nrhs // planes
        col_id = lax.axis_index("col")
        x_id = col_id % groups
        z_id = col_id // groups
        row_id = lax.axis_index("row")

        def lin(c, r):
            return c * n_row + r

        def reduce_col(partial_value):
            pieces = partial_value.reshape((groups, col_count) + partial_value.shape[1:])
            acc = lax.dynamic_index_in_dim(pieces, x_id, 0, keepdims=False)
            for s in range(1, groups):
                send = lax.dynamic_index_in_dim(pieces, (x_id + s) % groups, 0, keepdims=False)
                perm = [
                    (zz * groups + xx, zz * groups + (xx + s) % groups)
                    for zz in range(planes)
                    for xx in range(groups)
                ]
                acc = acc + lax.ppermute(send, "col", perm)
            bands = acc.reshape(col_count, planes, band, width)
            total = lax.dynamic_index_in_dim(bands, z_id, 1, keepdims=False)
            for s in range(1, planes):
                send = lax.dynamic_index_in_dim(bands, (z_id + s) % planes, 1, keepdims=False)
                perm = [
                    (zz * groups + xx, ((zz + s) % planes) * groups + xx)
                    for zz in range(planes)
                    for xx in range(groups)
                ]
                total = total + lax.ppermute(send, "col", perm)
            return total

        def deliver(piece):
            got = []
            for t in range(planes):
                perm = [
                    (lin(b * groups + xx, a), lin(a * groups + xx, (b + t) % n_row))
                    for a in range(n_row)
                    for b in range(planes)
                    for xx in range(groups)
                ]
                got.append(lax.ppermute(piece, ("col", "row"), perm))
            order = (row_id - jnp.arange(planes)) % planes
            slices = jnp.take(jnp.stack(got), order, axis=0)
            return slices.transpose(1, 0, 2, 3).reshape(col_count, nrhs, width)

        solved = []
        outputs = []
        for section in range(right_side.shape[0]):
            rhs_owned = lax.dynamic_slice(
                right_side[section], (x_id * col_count, z_id * band, 0), (col_count, band, width)
            )
            inv_owned = lax.dynamic_slice_in_dim(diag_inverse[section], x_id * col_count, col_count, 0)
            if section > 0:
                offset = section * (section - 1) // 2
                weights = pattern[offset : offset + section].astype(jnp.float32)
                blocks = lower_blocks[offset : offset + section]
                partial_value = contributions(
                    jnp.stack(solved[-1:]), blocks[section - 1 :], weights[section - 1 :]
                )
                if section > 1:
                    partial_value = partial_value + contributions(
                        jnp.stack(solved[:-1]), blocks[: section - 1], weights[: section - 1]
                    )
                residual = rhs_owned - reduce_col(partial_value)
            else:
                residual = rhs_owned
            segment = deliver(solve_rows(residual, inv_owned))
            outputs.append(segment)
            solved.append(segment.astype(jnp.bfloat16))
        return jnp.stack(outputs)

    return body


def solution(mesh):
    placed = (
        P(None, "row", None, None),
        P(None, "row", "col", None, None),
        P(None, "row", "col"),
        P(None, "row", None, None),
    )
    body = make_body(mesh.shape["col"], mesh.shape["row"])
    return jax.shard_map(
        body, mesh=mesh, in_specs=placed, out_specs=P(None, "col", None, None), check_vma=False
    )
```

```python
import jax
import jax.numpy as jnp
from jax import lax
from jax.sharding import PartitionSpec as P


def solve_rows(residual, inverse):
    return jnp.einsum(
        "pnb,pbd->pnd", residual, inverse.astype(jnp.float32), precision=lax.Precision.HIGHEST
    )


def contributions(earlier, blocks, weights):
    products = jnp.einsum("lcnb,lrcbd->lrcnd", earlier, blocks, preferred_element_type=jnp.float32)
    return jnp.sum(weights[:, :, :, None, None] * products, axis=(0, 2))


def ring_tree(size):
    rounds = []
    holders = list(range(size))
    while len(holders) > 1:
        step = []
        keep = []
        signed = sorted(holders, key=lambda d: (abs(d if d <= size // 2 else d - size), d))
        taken = set()
        for d in reversed(signed):
            if d in taken or d == 0:
                continue
            s = d if d <= size // 2 else d - size
            toward = s - 1 if s > 0 else s + 1
            while toward % size not in holders or toward % size in taken:
                toward = toward - 1 if toward > 0 else toward + 1
                if toward == 0:
                    break
            t = toward % size
            if t in taken or t == d:
                continue
            step.append((d, t))
            taken.add(d)
            taken.add(t)
        holders = [d for d in holders if d not in {a for a, _ in step}]
        rounds.append(step)
    return rounds


def make_body(n_col, n_row):
    def body(right_side, lower_blocks, pattern, diag_inverse):
        row_count = right_side.shape[1]
        col_count = pattern.shape[2]
        groups = row_count // col_count
        planes = n_col // groups
        col_id = lax.axis_index("col")
        row_id = lax.axis_index("row")
        x_id = col_id % groups
        z_id = col_id // groups
        is_root = z_id == row_id
        axes = ("col", "row")

        def lin(c, r):
            return c * n_row + r

        def reduce_to_root(partial_value):
            pieces = partial_value.reshape((groups, col_count) + partial_value.shape[1:])
            acc = lax.dynamic_index_in_dim(pieces, x_id, 0, keepdims=False)
            for s in range(1, groups):
                send = lax.dynamic_index_in_dim(pieces, (x_id + s) % groups, 0, keepdims=False)
                perm = [
                    (zz * groups + xx, zz * groups + (xx + s) % groups)
                    for zz in range(planes)
                    for xx in range(groups)
                ]
                acc = acc + lax.ppermute(send, "col", perm)
            for step in ring_tree(planes):
                perm = [
                    (
                        lin(((r + a) % planes) * groups + xx, r),
                        lin(((r + b) % planes) * groups + xx, r),
                    )
                    for r in range(n_row)
                    for xx in range(groups)
                    for a, b in step
                ]
                acc = acc + lax.ppermute(acc, axes, perm)
            return acc

        def broadcast_from_root(owned):
            val = jnp.where(is_root, owned, jnp.zeros_like(owned))
            bit = 1
            while bit < n_row:
                perm = [
                    (lin(z0 * groups + xx, z0 ^ d), lin(z0 * groups + xx, z0 ^ d ^ bit))
                    for z0 in range(planes)
                    for xx in range(groups)
                    for d in range(bit)
                ]
                val = val + lax.ppermute(val, axes, perm)
                bit *= 2
            return val

        solved = []
        outputs = []
        for section in range(right_side.shape[0]):
            rhs_owned = lax.dynamic_slice_in_dim(right_side[section], x_id * col_count, col_count, 0)
            inv_owned = lax.dynamic_slice_in_dim(diag_inverse[section], x_id * col_count, col_count, 0)
            if section > 0:
                offset = section * (section - 1) // 2
                weights = pattern[offset : offset + section].astype(jnp.float32)
                blocks = lower_blocks[offset : offset + section]
                partial_value = contributions(
                    jnp.stack(solved[-1:]), blocks[section - 1 :], weights[section - 1 :]
                )
                if section > 1:
                    partial_value = partial_value + contributions(
                        jnp.stack(solved[:-1]), blocks[: section - 1], weights[: section - 1]
                    )
                totals = reduce_to_root(partial_value)
                owned = solve_rows(rhs_owned - totals, inv_owned)
            else:
                owned = solve_rows(rhs_owned, inv_owned)
            segment = broadcast_from_root(owned)
            outputs.append(segment)
            solved.append(segment.astype(jnp.bfloat16))
        return jnp.stack(outputs)

    return body


def solution(mesh):
    placed = (
        P(None, "row", None, None),
        P(None, "row", "col", None, None),
        P(None, "row", "col"),
        P(None, "row", None, None),
    )
    body = make_body(mesh.shape["col"], mesh.shape["row"])
    return jax.shard_map(
        body, mesh=mesh, in_specs=placed, out_specs=P(None, "col", None, None), check_vma=False
    )
```

```python
import jax
import jax.numpy as jnp
from jax import lax
from jax.sharding import PartitionSpec as P


def solve_rows(residual, inverse):
    return jnp.einsum(
        "pnb,pbd->pnd", residual, inverse.astype(jnp.float32), precision=lax.Precision.HIGHEST
    )


def contributions(earlier, blocks, weights):
    products = jnp.einsum("lcnb,lrcbd->lrcnd", earlier, blocks, preferred_element_type=jnp.float32)
    return jnp.sum(weights[:, :, :, None, None] * products, axis=(0, 2))


def make_body(n_col, n_row):
    def body(right_side, lower_blocks, pattern, diag_inverse):
        row_count = right_side.shape[1]
        col_count = pattern.shape[2]
        groups = row_count // col_count
        planes = n_col // groups
        col_id = lax.axis_index("col")
        row_id = lax.axis_index("row")
        x_id = col_id % groups
        z_id = col_id // groups
        is_root = z_id == row_id
        axes = ("col", "row")

        def lin(c, r):
            return c * n_row + r

        def reduce_to_root(partial_value):
            pieces = partial_value.reshape((groups, col_count) + partial_value.shape[1:])
            acc = lax.dynamic_index_in_dim(pieces, x_id, 0, keepdims=False)
            for s in range(1, groups):
                send = lax.dynamic_index_in_dim(pieces, (x_id + s) % groups, 0, keepdims=False)
                perm = [
                    (zz * groups + xx, zz * groups + (xx + s) % groups)
                    for zz in range(planes)
                    for xx in range(groups)
                ]
                acc = acc + lax.ppermute(send, "col", perm)
            total = acc
            for s in range(1, planes):
                perm = [
                    (lin(((r + s) % planes) * groups + xx, r), lin(r * groups + xx, r))
                    for r in range(n_row)
                    for xx in range(groups)
                ]
                total = total + lax.ppermute(acc, axes, perm)
            return total

        def broadcast_from_root(owned):
            val = jnp.where(is_root, owned, jnp.zeros_like(owned))
            bit = 1
            while bit < n_row:
                perm = [
                    (lin(z0 * groups + xx, z0 ^ d), lin(z0 * groups + xx, z0 ^ d ^ bit))
                    for z0 in range(planes)
                    for xx in range(groups)
                    for d in range(bit)
                ]
                val = val + lax.ppermute(val, axes, perm)
                bit *= 2
            return val

        solved = []
        outputs = []
        for section in range(right_side.shape[0]):
            rhs_owned = lax.dynamic_slice_in_dim(right_side[section], x_id * col_count, col_count, 0)
            inv_owned = lax.dynamic_slice_in_dim(diag_inverse[section], x_id * col_count, col_count, 0)
            if section > 0:
                offset = section * (section - 1) // 2
                weights = pattern[offset : offset + section].astype(jnp.float32)
                blocks = lower_blocks[offset : offset + section]
                partial_value = contributions(
                    jnp.stack(solved[-1:]), blocks[section - 1 :], weights[section - 1 :]
                )
                if section > 1:
                    partial_value = partial_value + contributions(
                        jnp.stack(solved[:-1]), blocks[: section - 1], weights[: section - 1]
                    )
                totals = reduce_to_root(partial_value)
                owned = solve_rows(rhs_owned - totals, inv_owned)
            else:
                owned = solve_rows(rhs_owned, inv_owned)
            segment = broadcast_from_root(owned)
            outputs.append(segment)
            solved.append(segment.astype(jnp.bfloat16))
        return jnp.stack(outputs)

    return body


def solution(mesh):
    placed = (
        P(None, "row", None, None),
        P(None, "row", "col", None, None),
        P(None, "row", "col"),
        P(None, "row", None, None),
    )
    body = make_body(mesh.shape["col"], mesh.shape["row"])
    return jax.shard_map(
        body, mesh=mesh, in_specs=placed, out_specs=P(None, "col", None, None), check_vma=False
    )
```

```python
import jax
import jax.numpy as jnp
from jax import lax
from jax.sharding import PartitionSpec as P


def solve_rows(residual, inverse):
    return jnp.einsum(
        "pnb,pbd->pnd", residual, inverse.astype(jnp.float32), precision=lax.Precision.HIGHEST
    )


def contributions(earlier, blocks, weights):
    products = jnp.einsum("lcnb,lrcbd->lrcnd", earlier, blocks, preferred_element_type=jnp.float32)
    return jnp.sum(weights[:, :, :, None, None] * products, axis=(0, 2))


def make_body(n_col, n_row):
    def body(right_side, lower_blocks, pattern, diag_inverse):
        row_count = right_side.shape[1]
        col_count = pattern.shape[2]
        groups = row_count // col_count
        planes = n_col // groups
        col_id = lax.axis_index("col")
        row_id = lax.axis_index("row")
        x_id = col_id % groups
        z_id = col_id // groups
        is_root = z_id == row_id
        axes = ("col", "row")

        def lin(c, r):
            return c * n_row + r

        def reduce_to_root(partial_value):
            pieces = partial_value.reshape((groups, col_count) + partial_value.shape[1:])
            acc = lax.dynamic_index_in_dim(pieces, x_id, 0, keepdims=False)
            for s in range(1, groups):
                send = lax.dynamic_index_in_dim(pieces, (x_id + s) % groups, 0, keepdims=False)
                perm = [
                    (zz * groups + xx, zz * groups + (xx + s) % groups)
                    for zz in range(planes)
                    for xx in range(groups)
                ]
                acc = acc + lax.ppermute(send, "col", perm)
            total = acc
            for s in range(1, planes):
                perm = [
                    (lin(((r + s) % planes) * groups + xx, r), lin(r * groups + xx, r))
                    for r in range(n_row)
                    for xx in range(groups)
                ]
                total = total + lax.ppermute(acc, axes, perm)
            return total

        def broadcast_from_root(owned):
            val = jnp.where(is_root, owned, jnp.zeros_like(owned))
            bit = 1
            while bit < n_row:
                perm = [
                    (lin(z0 * groups + xx, z0 ^ d), lin(z0 * groups + xx, z0 ^ d ^ bit))
                    for z0 in range(planes)
                    for xx in range(groups)
                    for d in range(bit)
                ]
                val = val + lax.ppermute(val, axes, perm)
                bit *= 2
            return val

        nrhs = right_side.shape[2]
        chains = 2
        share = nrhs // chains
        solved = [[] for _ in range(chains)]
        outputs = [[] for _ in range(chains)]
        for section in range(right_side.shape[0]):
            inv_owned = lax.dynamic_slice_in_dim(diag_inverse[section], x_id * col_count, col_count, 0)
            offset = section * (section - 1) // 2
            weights = pattern[offset : offset + section].astype(jnp.float32)
            blocks = lower_blocks[offset : offset + section]
            for h in range(chains):
                rhs_owned = lax.dynamic_slice_in_dim(
                    right_side[section, :, h * share : (h + 1) * share], x_id * col_count, col_count, 0
                )
                if section > 0:
                    partial_value = contributions(
                        jnp.stack(solved[h][-1:]), blocks[section - 1 :], weights[section - 1 :]
                    )
                    if section > 1:
                        partial_value = partial_value + contributions(
                            jnp.stack(solved[h][:-1]), blocks[: section - 1], weights[: section - 1]
                        )
                    totals = reduce_to_root(partial_value)
                    owned = solve_rows(rhs_owned - totals, inv_owned)
                else:
                    owned = solve_rows(rhs_owned, inv_owned)
                segment = broadcast_from_root(owned)
                outputs[h].append(segment)
                solved[h].append(segment.astype(jnp.bfloat16))
        return jnp.concatenate([jnp.stack(o) for o in outputs], axis=2)

    return body


def solution(mesh):
    placed = (
        P(None, "row", None, None),
        P(None, "row", "col", None, None),
        P(None, "row", "col"),
        P(None, "row", None, None),
    )
    body = make_body(mesh.shape["col"], mesh.shape["row"])
    return jax.shard_map(
        body, mesh=mesh, in_specs=placed, out_specs=P(None, "col", None, None), check_vma=False
    )
```

```python
import jax
import jax.numpy as jnp
from jax import lax
from jax.sharding import PartitionSpec as P


def solve_rows(residual, inverse):
    return jnp.einsum(
        "pnb,pbd->pnd", residual, inverse.astype(jnp.float32), precision=lax.Precision.HIGHEST
    )


def contributions(earlier, blocks, weights):
    products = jnp.einsum("lcnb,lrcbd->lrcnd", earlier, blocks, preferred_element_type=jnp.float32)
    return jnp.sum(weights[:, :, :, None, None] * products, axis=(0, 2))


def make_body(n_col, n_row):
    def body(right_side, lower_blocks, pattern, diag_inverse):
        row_count = right_side.shape[1]
        col_count = pattern.shape[2]
        groups = row_count // col_count
        planes = n_col // groups
        col_id = lax.axis_index("col")
        row_id = lax.axis_index("row")
        x_id = col_id % groups
        z_id = col_id // groups
        is_root = z_id == row_id
        axes = ("col", "row")

        def lin(c, r):
            return c * n_row + r

        def reduce_to_root(partial_value):
            pieces = partial_value.reshape((groups, col_count) + partial_value.shape[1:])
            acc = lax.dynamic_index_in_dim(pieces, x_id, 0, keepdims=False)
            for s in range(1, groups):
                send = lax.dynamic_index_in_dim(pieces, (x_id + s) % groups, 0, keepdims=False)
                perm = [
                    (zz * groups + xx, zz * groups + (xx + s) % groups)
                    for zz in range(planes)
                    for xx in range(groups)
                ]
                acc = acc + lax.ppermute(send, "col", perm)
            half = planes // 2
            total = acc
            for j in range(1, half):
                perm = [
                    (
                        lin(((r + a) % planes) * groups + xx, r),
                        lin(((r + b) % planes) * groups + xx, r),
                    )
                    for r in range(n_row)
                    for xx in range(groups)
                    for a, b in ((-j, 0), (1 + j, 1))
                ]
                total = total + lax.ppermute(acc, axes, perm)
            perm = [
                (lin(((r + 1) % planes) * groups + xx, r), lin(r * groups + xx, r))
                for r in range(n_row)
                for xx in range(groups)
            ]
            return total + lax.ppermute(total, axes, perm)

        def broadcast_from_root(owned):
            val = jnp.where(is_root, owned, jnp.zeros_like(owned))
            bit = 1
            while bit < n_row:
                perm = [
                    (lin(z0 * groups + xx, z0 ^ d), lin(z0 * groups + xx, z0 ^ d ^ bit))
                    for z0 in range(planes)
                    for xx in range(groups)
                    for d in range(bit)
                ]
                val = val + lax.ppermute(val, axes, perm)
                bit *= 2
            return val

        solved = []
        outputs = []
        for section in range(right_side.shape[0]):
            rhs_owned = lax.dynamic_slice_in_dim(right_side[section], x_id * col_count, col_count, 0)
            inv_owned = lax.dynamic_slice_in_dim(diag_inverse[section], x_id * col_count, col_count, 0)
            if section > 0:
                offset = section * (section - 1) // 2
                weights = pattern[offset : offset + section].astype(jnp.float32)
                blocks = lower_blocks[offset : offset + section]
                partial_value = contributions(
                    jnp.stack(solved[-1:]), blocks[section - 1 :], weights[section - 1 :]
                )
                if section > 1:
                    partial_value = partial_value + contributions(
                        jnp.stack(solved[:-1]), blocks[: section - 1], weights[: section - 1]
                    )
                totals = reduce_to_root(partial_value)
                owned = solve_rows(rhs_owned - totals, inv_owned)
            else:
                owned = solve_rows(rhs_owned, inv_owned)
            segment = broadcast_from_root(owned)
            outputs.append(segment)
            solved.append(segment.astype(jnp.bfloat16))
        return jnp.stack(outputs)

    return body


def solution(mesh):
    placed = (
        P(None, "row", None, None),
        P(None, "row", "col", None, None),
        P(None, "row", "col"),
        P(None, "row", None, None),
    )
    body = make_body(mesh.shape["col"], mesh.shape["row"])
    return jax.shard_map(
        body, mesh=mesh, in_specs=placed, out_specs=P(None, "col", None, None), check_vma=False
    )
```

```python
import jax
import jax.numpy as jnp
from jax import lax
from jax.sharding import PartitionSpec as P


def solve_rows(residual, inverse):
    return jnp.einsum(
        "pnb,pbd->pnd", residual, inverse.astype(jnp.float32), precision=lax.Precision.HIGHEST
    )


def contributions(earlier, blocks, weights):
    products = jnp.einsum("lcnb,lrcbd->lrcnd", earlier, blocks, preferred_element_type=jnp.float32)
    return jnp.sum(weights[:, :, :, None, None] * products, axis=(0, 2))


def make_body(n_col, n_row):
    def body(right_side, lower_blocks, pattern, diag_inverse):
        row_count = right_side.shape[1]
        col_count = pattern.shape[2]
        groups = row_count // col_count
        planes = n_col // groups
        col_id = lax.axis_index("col")
        row_id = lax.axis_index("row")
        x_id = col_id % groups
        z_id = col_id // groups
        is_root = z_id == row_id
        axes = ("col", "row")

        def lin(c, r):
            return c * n_row + r

        def reduce_to_root(partial_value):
            pieces = partial_value.reshape((groups, col_count) + partial_value.shape[1:])
            acc = lax.dynamic_index_in_dim(pieces, x_id, 0, keepdims=False)
            for s in range(1, groups):
                send = lax.dynamic_index_in_dim(pieces, (x_id + s) % groups, 0, keepdims=False)
                perm = [
                    (zz * groups + xx, zz * groups + (xx + s) % groups)
                    for zz in range(planes)
                    for xx in range(groups)
                ]
                acc = acc + lax.ppermute(send, "col", perm)
            total = acc
            for s in range(1, planes):
                perm = [
                    (lin(((r + s) % planes) * groups + xx, r), lin(r * groups + xx, r))
                    for r in range(n_row)
                    for xx in range(groups)
                ]
                total = total + lax.ppermute(acc, axes, perm)
            return total

        def broadcast_from_root(owned):
            val = jnp.where(is_root, owned, jnp.zeros_like(owned))
            if n_row == 8:
                for rounds in (((0, 1),), ((0, 2),)), (((0, 4), (1, 5), (2, 6)), ((1, 3), (2, 7))):
                    got = val
                    for pairs in rounds:
                        perm = [
                            (lin(z0 * groups + xx, z0 ^ a), lin(z0 * groups + xx, z0 ^ b))
                            for z0 in range(planes)
                            for xx in range(groups)
                            for a, b in pairs
                        ]
                        got = got + lax.ppermute(val, axes, perm)
                    val = got
                return val
            bit = 1
            while bit < n_row:
                perm = [
                    (lin(z0 * groups + xx, z0 ^ d), lin(z0 * groups + xx, z0 ^ d ^ bit))
                    for z0 in range(planes)
                    for xx in range(groups)
                    for d in range(bit)
                ]
                val = val + lax.ppermute(val, axes, perm)
                bit *= 2
            return val

        solved = []
        outputs = []
        for section in range(right_side.shape[0]):
            rhs_owned = lax.dynamic_slice_in_dim(right_side[section], x_id * col_count, col_count, 0)
            inv_owned = lax.dynamic_slice_in_dim(diag_inverse[section], x_id * col_count, col_count, 0)
            if section > 0:
                offset = section * (section - 1) // 2
                weights = pattern[offset : offset + section].astype(jnp.float32)
                blocks = lower_blocks[offset : offset + section]
                partial_value = contributions(
                    jnp.stack(solved[-1:]), blocks[section - 1 :], weights[section - 1 :]
                )
                if section > 1:
                    partial_value = partial_value + contributions(
                        jnp.stack(solved[:-1]), blocks[: section - 1], weights[: section - 1]
                    )
                totals = reduce_to_root(partial_value)
                owned = solve_rows(rhs_owned - totals, inv_owned)
            else:
                owned = solve_rows(rhs_owned, inv_owned)
            segment = broadcast_from_root(owned)
            outputs.append(segment)
            solved.append(segment.astype(jnp.bfloat16))
        return jnp.stack(outputs)

    return body


def solution(mesh):
    placed = (
        P(None, "row", None, None),
        P(None, "row", "col", None, None),
        P(None, "row", "col"),
        P(None, "row", None, None),
    )
    body = make_body(mesh.shape["col"], mesh.shape["row"])
    return jax.shard_map(
        body, mesh=mesh, in_specs=placed, out_specs=P(None, "col", None, None), check_vma=False
    )
```

```python
import jax
import jax.numpy as jnp
from jax import lax
from jax.sharding import PartitionSpec as P


def solve_rows(residual, inverse):
    high = residual.astype(jnp.bfloat16)
    rest = residual - high.astype(jnp.float32)
    middle = rest.astype(jnp.bfloat16)
    low = (rest - middle.astype(jnp.float32)).astype(jnp.bfloat16)
    out = None
    for part in (low, middle, high):
        term = jnp.einsum("pnb,pbd->pnd", part, inverse, preferred_element_type=jnp.float32)
        out = term if out is None else out + term
    return out


def contributions(earlier, blocks, weights):
    products = jnp.einsum("lcnb,lrcbd->lrcnd", earlier, blocks, preferred_element_type=jnp.float32)
    return jnp.sum(weights[:, :, :, None, None] * products, axis=(0, 2))


def make_body(n_col, n_row):
    def body(right_side, lower_blocks, pattern, diag_inverse):
        row_count = right_side.shape[1]
        col_count = pattern.shape[2]
        groups = row_count // col_count
        planes = n_col // groups
        col_id = lax.axis_index("col")
        row_id = lax.axis_index("row")
        x_id = col_id % groups
        z_id = col_id // groups
        is_root = z_id == row_id
        axes = ("col", "row")

        def lin(c, r):
            return c * n_row + r

        def reduce_to_root(partial_value):
            pieces = partial_value.reshape((groups, col_count) + partial_value.shape[1:])
            acc = lax.dynamic_index_in_dim(pieces, x_id, 0, keepdims=False)
            for s in range(1, groups):
                send = lax.dynamic_index_in_dim(pieces, (x_id + s) % groups, 0, keepdims=False)
                perm = [
                    (zz * groups + xx, zz * groups + (xx + s) % groups)
                    for zz in range(planes)
                    for xx in range(groups)
                ]
                acc = acc + lax.ppermute(send, "col", perm)
            total = acc
            for s in range(1, planes):
                perm = [
                    (lin(((r + s) % planes) * groups + xx, r), lin(r * groups + xx, r))
                    for r in range(n_row)
                    for xx in range(groups)
                ]
                total = total + lax.ppermute(acc, axes, perm)
            return total

        def broadcast_from_root(owned):
            val = jnp.where(is_root, owned, jnp.zeros_like(owned))
            if n_row == 8:
                for rounds in (((0, 1),), ((0, 2),)), (((0, 4), (1, 5), (2, 6)), ((1, 3), (2, 7))):
                    got = val
                    for pairs in rounds:
                        perm = [
                            (lin(z0 * groups + xx, z0 ^ a), lin(z0 * groups + xx, z0 ^ b))
                            for z0 in range(planes)
                            for xx in range(groups)
                            for a, b in pairs
                        ]
                        got = got + lax.ppermute(val, axes, perm)
                    val = got
                return val
            bit = 1
            while bit < n_row:
                perm = [
                    (lin(z0 * groups + xx, z0 ^ d), lin(z0 * groups + xx, z0 ^ d ^ bit))
                    for z0 in range(planes)
                    for xx in range(groups)
                    for d in range(bit)
                ]
                val = val + lax.ppermute(val, axes, perm)
                bit *= 2
            return val

        solved = []
        outputs = []
        for section in range(right_side.shape[0]):
            rhs_owned = lax.dynamic_slice_in_dim(right_side[section], x_id * col_count, col_count, 0)
            inv_owned = lax.dynamic_slice_in_dim(diag_inverse[section], x_id * col_count, col_count, 0)
            if section > 0:
                offset = section * (section - 1) // 2
                weights = pattern[offset : offset + section].astype(jnp.float32)
                blocks = lower_blocks[offset : offset + section]
                partial_value = contributions(
                    jnp.stack(solved[-1:]), blocks[section - 1 :], weights[section - 1 :]
                )
                if section > 1:
                    partial_value = partial_value + contributions(
                        jnp.stack(solved[:-1]), blocks[: section - 1], weights[: section - 1]
                    )
                totals = reduce_to_root(partial_value)
                owned = solve_rows(rhs_owned - totals, inv_owned)
            else:
                owned = solve_rows(rhs_owned, inv_owned)
            segment = broadcast_from_root(owned)
            outputs.append(segment)
            solved.append(segment.astype(jnp.bfloat16))
        return jnp.stack(outputs)

    return body


def solution(mesh):
    placed = (
        P(None, "row", None, None),
        P(None, "row", "col", None, None),
        P(None, "row", "col"),
        P(None, "row", None, None),
    )
    body = make_body(mesh.shape["col"], mesh.shape["row"])
    return jax.shard_map(
        body, mesh=mesh, in_specs=placed, out_specs=P(None, "col", None, None), check_vma=False
    )
```

```python
import jax
import jax.numpy as jnp
from jax import lax
from jax.sharding import PartitionSpec as P


def solve_rows(residual, inverse):
    return jnp.einsum(
        "pnb,pbd->pnd", residual, inverse.astype(jnp.float32), precision=lax.Precision.HIGHEST
    )


def contributions(earlier, blocks, weights):
    products = jnp.einsum("lcnb,lrcbd->lrcnd", earlier, blocks, preferred_element_type=jnp.float32)
    return jnp.sum(weights[:, :, :, None, None] * products, axis=(0, 2))


def make_body(n_col, n_row):
    def body(right_side, lower_blocks, pattern, diag_inverse):
        row_count = right_side.shape[1]
        col_count = pattern.shape[2]
        groups = row_count // col_count
        planes = n_col // groups
        col_id = lax.axis_index("col")
        row_id = lax.axis_index("row")
        x_id = col_id % groups
        z_id = col_id // groups
        is_root = z_id == row_id
        axes = ("col", "row")

        def lin(c, r):
            return c * n_row + r

        def reduce_to_root(partial_value):
            pieces = partial_value.reshape((groups, col_count) + partial_value.shape[1:])
            acc = lax.dynamic_index_in_dim(pieces, x_id, 0, keepdims=False)
            for s in range(1, groups):
                send = lax.dynamic_index_in_dim(pieces, (x_id + s) % groups, 0, keepdims=False)
                perm = [
                    (zz * groups + xx, zz * groups + (xx + s) % groups)
                    for zz in range(planes)
                    for xx in range(groups)
                ]
                acc = acc + lax.ppermute(send, "col", perm)
            total = acc
            for s in sorted(range(1, planes), key=lambda d: (-min(d, planes - d), d)):
                perm = [
                    (lin(((r + s) % planes) * groups + xx, r), lin(r * groups + xx, r))
                    for r in range(n_row)
                    for xx in range(groups)
                ]
                total = total + lax.ppermute(acc, axes, perm)
            return total

        def broadcast_from_root(owned):
            val = jnp.where(is_root, owned, jnp.zeros_like(owned))
            if n_row == 8:
                for rounds in (((0, 1),), ((0, 2),)), (((0, 4), (1, 5), (2, 6)), ((1, 3), (2, 7))):
                    got = val
                    for pairs in rounds:
                        perm = [
                            (lin(z0 * groups + xx, z0 ^ a), lin(z0 * groups + xx, z0 ^ b))
                            for z0 in range(planes)
                            for xx in range(groups)
                            for a, b in pairs
                        ]
                        got = got + lax.ppermute(val, axes, perm)
                    val = got
                return val
            bit = 1
            while bit < n_row:
                perm = [
                    (lin(z0 * groups + xx, z0 ^ d), lin(z0 * groups + xx, z0 ^ d ^ bit))
                    for z0 in range(planes)
                    for xx in range(groups)
                    for d in range(bit)
                ]
                val = val + lax.ppermute(val, axes, perm)
                bit *= 2
            return val

        solved = []
        outputs = []
        for section in range(right_side.shape[0]):
            rhs_owned = lax.dynamic_slice_in_dim(right_side[section], x_id * col_count, col_count, 0)
            inv_owned = lax.dynamic_slice_in_dim(diag_inverse[section], x_id * col_count, col_count, 0)
            if section > 0:
                offset = section * (section - 1) // 2
                weights = pattern[offset : offset + section].astype(jnp.float32)
                blocks = lower_blocks[offset : offset + section]
                partial_value = contributions(
                    jnp.stack(solved[-1:]), blocks[section - 1 :], weights[section - 1 :]
                )
                if section > 1:
                    partial_value = partial_value + contributions(
                        jnp.stack(solved[:-1]), blocks[: section - 1], weights[: section - 1]
                    )
                totals = reduce_to_root(partial_value)
                owned = solve_rows(rhs_owned - totals, inv_owned)
            else:
                owned = solve_rows(rhs_owned, inv_owned)
            segment = broadcast_from_root(owned)
            outputs.append(segment)
            solved.append(segment.astype(jnp.bfloat16))
        return jnp.stack(outputs)

    return body


def solution(mesh):
    placed = (
        P(None, "row", None, None),
        P(None, "row", "col", None, None),
        P(None, "row", "col"),
        P(None, "row", None, None),
    )
    body = make_body(mesh.shape["col"], mesh.shape["row"])
    return jax.shard_map(
        body, mesh=mesh, in_specs=placed, out_specs=P(None, "col", None, None), check_vma=False
    )
```

```python
import jax
import jax.numpy as jnp
from jax import lax
from jax.sharding import PartitionSpec as P


def solve_rows(residual, inverse):
    return jnp.einsum(
        "pnb,pbd->pnd", residual, inverse.astype(jnp.float32), precision=lax.Precision.HIGHEST
    )


def contributions(earlier, blocks, weights):
    products = jnp.einsum("lcnb,lrcbd->lrcnd", earlier, blocks, preferred_element_type=jnp.float32)
    return jnp.sum(weights[:, :, :, None, None] * products, axis=(0, 2))


def make_body(n_col, n_row):
    def body(right_side, lower_blocks, pattern, diag_inverse):
        row_count = right_side.shape[1]
        col_count = pattern.shape[2]
        groups = row_count // col_count
        planes = n_col // groups
        col_id = lax.axis_index("col")
        row_id = lax.axis_index("row")
        x_id = col_id % groups
        z_id = col_id // groups
        is_root = z_id == row_id
        axes = ("col", "row")

        def lin(c, r):
            return c * n_row + r

        def reduce_to_root(partial_value):
            pieces = partial_value.reshape((groups, col_count) + partial_value.shape[1:])
            acc = lax.dynamic_index_in_dim(pieces, x_id, 0, keepdims=False)
            for s in sorted(range(1, groups), key=lambda d: (-min(d, groups - d), d)):
                send = lax.dynamic_index_in_dim(pieces, (x_id + s) % groups, 0, keepdims=False)
                perm = [
                    (zz * groups + xx, zz * groups + (xx + s) % groups)
                    for zz in range(planes)
                    for xx in range(groups)
                ]
                acc = acc + lax.ppermute(send, "col", perm)
            total = acc
            for s in sorted(range(1, planes), key=lambda d: (-min(d, planes - d), d)):
                perm = [
                    (lin(((r + s) % planes) * groups + xx, r), lin(r * groups + xx, r))
                    for r in range(n_row)
                    for xx in range(groups)
                ]
                total = total + lax.ppermute(acc, axes, perm)
            return total

        def broadcast_from_root(owned):
            val = jnp.where(is_root, owned, jnp.zeros_like(owned))
            if n_row == 8:
                for rounds in (((0, 2),), ((0, 1),)), (((0, 4), (1, 5), (2, 6)), ((1, 3), (2, 7))):
                    got = val
                    for pairs in rounds:
                        perm = [
                            (lin(z0 * groups + xx, z0 ^ a), lin(z0 * groups + xx, z0 ^ b))
                            for z0 in range(planes)
                            for xx in range(groups)
                            for a, b in pairs
                        ]
                        got = got + lax.ppermute(val, axes, perm)
                    val = got
                return val
            bit = 1
            while bit < n_row:
                perm = [
                    (lin(z0 * groups + xx, z0 ^ d), lin(z0 * groups + xx, z0 ^ d ^ bit))
                    for z0 in range(planes)
                    for xx in range(groups)
                    for d in range(bit)
                ]
                val = val + lax.ppermute(val, axes, perm)
                bit *= 2
            return val

        solved = []
        outputs = []
        for section in range(right_side.shape[0]):
            rhs_owned = lax.dynamic_slice_in_dim(right_side[section], x_id * col_count, col_count, 0)
            inv_owned = lax.dynamic_slice_in_dim(diag_inverse[section], x_id * col_count, col_count, 0)
            if section > 0:
                offset = section * (section - 1) // 2
                weights = pattern[offset : offset + section].astype(jnp.float32)
                blocks = lower_blocks[offset : offset + section]
                partial_value = contributions(
                    jnp.stack(solved[-1:]), blocks[section - 1 :], weights[section - 1 :]
                )
                if section > 1:
                    partial_value = partial_value + contributions(
                        jnp.stack(solved[:-1]), blocks[: section - 1], weights[: section - 1]
                    )
                totals = reduce_to_root(partial_value)
                owned = solve_rows(rhs_owned - totals, inv_owned)
            else:
                owned = solve_rows(rhs_owned, inv_owned)
            segment = broadcast_from_root(owned)
            outputs.append(segment)
            solved.append(segment.astype(jnp.bfloat16))
        return jnp.stack(outputs)

    return body


def solution(mesh):
    placed = (
        P(None, "row", None, None),
        P(None, "row", "col", None, None),
        P(None, "row", "col"),
        P(None, "row", None, None),
    )
    body = make_body(mesh.shape["col"], mesh.shape["row"])
    return jax.shard_map(
        body, mesh=mesh, in_specs=placed, out_specs=P(None, "col", None, None), check_vma=False
    )
```

```python
import jax
import jax.numpy as jnp
from jax import lax
from jax.sharding import PartitionSpec as P


def solve_rows(residual, inverse):
    return jnp.einsum(
        "pnb,pbd->pnd", residual, inverse.astype(jnp.float32), precision=lax.Precision.HIGHEST
    )


def contributions(earlier, blocks, weights):
    products = jnp.einsum("lcnb,lrcbd->lrcnd", earlier, blocks, preferred_element_type=jnp.float32)
    return jnp.sum(weights[:, :, :, None, None] * products, axis=(0, 2))


def make_body(n_col, n_row):
    def body(right_side, lower_blocks, pattern, diag_inverse):
        row_count = right_side.shape[1]
        col_count = pattern.shape[2]
        groups = row_count // col_count
        planes = n_col // groups
        col_id = lax.axis_index("col")
        row_id = lax.axis_index("row")
        x_id = col_id % groups
        z_id = col_id // groups
        is_root = z_id == row_id
        axes = ("col", "row")

        def lin(c, r):
            return c * n_row + r

        def reduce_to_root(partial_value):
            pieces = partial_value.reshape((groups, col_count) + partial_value.shape[1:])
            acc = lax.dynamic_index_in_dim(pieces, x_id, 0, keepdims=False)
            for s in sorted(range(1, groups), key=lambda d: (-min(d, groups - d), d)):
                send = lax.dynamic_index_in_dim(pieces, (x_id + s) % groups, 0, keepdims=False)
                perm = [
                    (zz * groups + xx, zz * groups + (xx + s) % groups)
                    for zz in range(planes)
                    for xx in range(groups)
                ]
                acc = acc + lax.ppermute(send, "col", perm)
            total = acc
            for s in sorted(range(1, planes), key=lambda d: (-min(d, planes - d), d)):
                perm = [
                    (lin(((r + s) % planes) * groups + xx, r), lin(r * groups + xx, r))
                    for r in range(n_row)
                    for xx in range(groups)
                ]
                total = total + lax.ppermute(acc, axes, perm)
            return total

        def broadcast_from_root(owned):
            val = jnp.where(is_root, owned, jnp.zeros_like(owned))
            if n_row == 8:
                for rounds in (((0, 4),), ((0, 2),), ((0, 1),)), (((1, 3), (4, 5), (2, 6), (0, 7)),):
                    got = val
                    for pairs in rounds:
                        perm = [
                            (lin(z0 * groups + xx, z0 ^ a), lin(z0 * groups + xx, z0 ^ b))
                            for z0 in range(planes)
                            for xx in range(groups)
                            for a, b in pairs
                        ]
                        got = got + lax.ppermute(val, axes, perm)
                    val = got
                return val
            bit = 1
            while bit < n_row:
                perm = [
                    (lin(z0 * groups + xx, z0 ^ d), lin(z0 * groups + xx, z0 ^ d ^ bit))
                    for z0 in range(planes)
                    for xx in range(groups)
                    for d in range(bit)
                ]
                val = val + lax.ppermute(val, axes, perm)
                bit *= 2
            return val

        solved = []
        outputs = []
        for section in range(right_side.shape[0]):
            rhs_owned = lax.dynamic_slice_in_dim(right_side[section], x_id * col_count, col_count, 0)
            inv_owned = lax.dynamic_slice_in_dim(diag_inverse[section], x_id * col_count, col_count, 0)
            if section > 0:
                offset = section * (section - 1) // 2
                weights = pattern[offset : offset + section].astype(jnp.float32)
                blocks = lower_blocks[offset : offset + section]
                partial_value = contributions(
                    jnp.stack(solved[-1:]), blocks[section - 1 :], weights[section - 1 :]
                )
                if section > 1:
                    partial_value = partial_value + contributions(
                        jnp.stack(solved[:-1]), blocks[: section - 1], weights[: section - 1]
                    )
                totals = reduce_to_root(partial_value)
                owned = solve_rows(rhs_owned - totals, inv_owned)
            else:
                owned = solve_rows(rhs_owned, inv_owned)
            segment = broadcast_from_root(owned)
            outputs.append(segment)
            solved.append(segment.astype(jnp.bfloat16))
        return jnp.stack(outputs)

    return body


def solution(mesh):
    placed = (
        P(None, "row", None, None),
        P(None, "row", "col", None, None),
        P(None, "row", "col"),
        P(None, "row", None, None),
    )
    body = make_body(mesh.shape["col"], mesh.shape["row"])
    return jax.shard_map(
        body, mesh=mesh, in_specs=placed, out_specs=P(None, "col", None, None), check_vma=False
    )
```

```python
import jax
import jax.numpy as jnp
from jax import lax
from jax.sharding import PartitionSpec as P


def solve_rows(residual, inverse):
    return jnp.einsum(
        "pnb,pbd->pnd", residual, inverse.astype(jnp.float32), precision=lax.Precision.HIGHEST
    )


def contributions(earlier, blocks, weights):
    products = jnp.einsum("lcnb,lrcbd->lrcnd", earlier, blocks, preferred_element_type=jnp.float32)
    return jnp.sum(weights[:, :, :, None, None] * products, axis=(0, 2))


def make_body(n_col, n_row):
    def body(right_side, lower_blocks, pattern, diag_inverse):
        row_count = right_side.shape[1]
        col_count = pattern.shape[2]
        groups = row_count // col_count
        planes = n_col // groups
        col_id = lax.axis_index("col")
        row_id = lax.axis_index("row")
        x_id = col_id % groups
        z_id = col_id // groups
        is_root = z_id == row_id
        axes = ("col", "row")

        def lin(c, r):
            return c * n_row + r

        def reduce_to_root(partial_value):
            pieces = partial_value.reshape((groups, col_count) + partial_value.shape[1:])
            acc = lax.dynamic_index_in_dim(pieces, x_id, 0, keepdims=False)
            for s in sorted(range(1, groups), key=lambda d: (-min(d, groups - d), d)):
                send = lax.dynamic_index_in_dim(pieces, (x_id + s) % groups, 0, keepdims=False)
                perm = [
                    (zz * groups + xx, zz * groups + (xx + s) % groups)
                    for zz in range(planes)
                    for xx in range(groups)
                ]
                acc = acc + lax.ppermute(send, "col", perm)
            total = acc
            for s in sorted(range(1, planes), key=lambda d: (-min(d, planes - d), d)):
                perm = [
                    (lin(((r + s) % planes) * groups + xx, r), lin(r * groups + xx, r))
                    for r in range(n_row)
                    for xx in range(groups)
                ]
                total = total + lax.ppermute(acc, axes, perm)
            return total

        def broadcast_from_root(owned):
            val = jnp.where(is_root, owned, jnp.zeros_like(owned))
            if n_row == 8:
                for rounds in (((0, 4),), ((0, 1),)), (((0, 2), (1, 3), (4, 6)), ((4, 5), (1, 7))):
                    got = val
                    for pairs in rounds:
                        perm = [
                            (lin(z0 * groups + xx, z0 ^ a), lin(z0 * groups + xx, z0 ^ b))
                            for z0 in range(planes)
                            for xx in range(groups)
                            for a, b in pairs
                        ]
                        got = got + lax.ppermute(val, axes, perm)
                    val = got
                return val
            bit = 1
            while bit < n_row:
                perm = [
                    (lin(z0 * groups + xx, z0 ^ d), lin(z0 * groups + xx, z0 ^ d ^ bit))
                    for z0 in range(planes)
                    for xx in range(groups)
                    for d in range(bit)
                ]
                val = val + lax.ppermute(val, axes, perm)
                bit *= 2
            return val

        solved = []
        outputs = []
        for section in range(right_side.shape[0]):
            rhs_owned = lax.dynamic_slice_in_dim(right_side[section], x_id * col_count, col_count, 0)
            inv_owned = lax.dynamic_slice_in_dim(diag_inverse[section], x_id * col_count, col_count, 0)
            if section > 0:
                offset = section * (section - 1) // 2
                weights = pattern[offset : offset + section].astype(jnp.float32)
                blocks = lower_blocks[offset : offset + section]
                partial_value = contributions(
                    jnp.stack(solved[-1:]), blocks[section - 1 :], weights[section - 1 :]
                )
                if section > 1:
                    partial_value = partial_value + contributions(
                        jnp.stack(solved[:-1]), blocks[: section - 1], weights[: section - 1]
                    )
                totals = reduce_to_root(partial_value)
                owned = solve_rows(rhs_owned - totals, inv_owned)
            else:
                owned = solve_rows(rhs_owned, inv_owned)
            segment = broadcast_from_root(owned)
            outputs.append(segment)
            solved.append(segment.astype(jnp.bfloat16))
        return jnp.stack(outputs)

    return body


def solution(mesh):
    placed = (
        P(None, "row", None, None),
        P(None, "row", "col", None, None),
        P(None, "row", "col"),
        P(None, "row", None, None),
    )
    body = make_body(mesh.shape["col"], mesh.shape["row"])
    return jax.shard_map(
        body, mesh=mesh, in_specs=placed, out_specs=P(None, "col", None, None), check_vma=False
    )
```
